128 devices in a mesh: row: 16 (over z_lo, x, core), col: 8 (over y, z_hi).
Axes of the slice: x: 4, y: 4, z: 4 (z_hi: 2, z_lo: 2; z = z_hi * 2 + z_lo), core: 2. Of those that a mesh axis runs over, the one named last changes fastest.
Arguments:
- shared_rows: float32 [2048, 16384], P('row', 'col'), may hold values from -0.125 to 0.125
- event_counts: int32 [16], replicated, may hold values from 32 to 128, as said below
- ridge: float32 [16384], P('col'), may hold values from 0.5 to 2
- items: float32 [1024, 16384], P('row', 'col'), may hold values from -6 to 6
- cand_ids: int32 [512], replicated, may hold values from 0 to 1023
- theta: float32 [16384], P('col'), may hold values from -0.046875 to 0.046875
Outputs:
- gram_tile: float32 [16384, 16384], P('row', 'col')
- scores: float32 [512], replicated
The draws below stay inside these ranges and needn't reach their ends.
Inputs may be any that keep to these rules, and one draw needn't show every extreme that they name: event_counts[s] counts the live slots at the start of row shard s's 128 slots; some shard is full.
All inputs are finite; a program needn't handle non-finite values.
Results may differ from the reference program's by a relative error of at most 0.000068.
Values sent between devices are 32-bit elements; how exact they have to be, the bound alone decides.
No kernel may reach another device: no remote copies, remote signals or barrier semaphores. Data moves between devices by JAX's collectives and lax.ppermute only.
A program may use at most 128 MiB of HBM per device.

```python
import math
import jax
import jax.numpy as jnp
from jax import lax

F = 16384
EV_DEV = 128
CANDS = 512
EVENTS = 2048
ITEMS = 1024
N_ROW = 16


def draw_event_counts(key, part):
    counts = jax.random.randint(key, (N_ROW,), EV_DEV // 4, EV_DEV + 1)
    where_full = jax.random.randint(jax.random.fold_in(key, 7), (), 0, N_ROW)
    return counts.at[where_full].set(EV_DEV).astype(jnp.int32)


def with_ends(entries, key, low, largest):
    longest = entries.shape.index(max(entries.shape))
    spots = []
    for shift in (0, 1):
        where = [jax.random.randint(jax.random.fold_in(key, axis), (), 0, length) for axis, length in enumerate(entries.shape)]
        where[longest] = (where[longest] + shift) % entries.shape[longest]
        spots.append(tuple(where))
    return entries.at[spots[0]].set(low).at[spots[1]].set(largest)


def steps_of(key, extent, pieces, least, high):
    factor_of = 1.0
    for axis_at, blocks in pieces:
        heights = jax.random.uniform(jax.random.fold_in(jax.random.fold_in(key, 6), axis_at), (blocks,), jnp.float32, least / len(pieces), high / len(pieces))
        factor_of = factor_of * jnp.repeat(jnp.exp(heights), extent[axis_at] // blocks).reshape((-1,) + (1,) * (len(extent) - 1 - axis_at))
    return factor_of


def bell_draw(key, shape, deviation, reach, split=(), held_as=jnp.bfloat16):
    gain = steps_of(key, shape, split, -0.22, 0.18) if split else 1.0
    array = jax.random.normal(key, shape, jnp.float32) * deviation * gain
    return jnp.minimum(jnp.maximum(array, -reach), reach).astype(held_as)


def setup_inputs(seed: int = 0) -> dict:
    arg_keys = jax.random.split(jax.random.key(seed), 7)
    shared_rows = bell_draw(arg_keys[0], (EVENTS, F), EVENTS ** -0.5, 0.125, ((0, 16), (1, 8)), jnp.float32)
    event_counts = draw_event_counts(jax.random.fold_in(arg_keys[6], 71), 0)
    ridge = jnp.clip(jnp.exp(math.log(2.0) - 1.3862944 * jax.random.uniform(arg_keys[2], (F,), jnp.float32) ** steps_of(arg_keys[2], (F,), ((0, 8),), -0.2, 0.2)), 0.5, 2.0)
    items = bell_draw(arg_keys[3], (ITEMS, F), 1.0, 6.0, ((0, 16), (1, 8)), jnp.float32)
    cand_ids = with_ends(jax.random.randint(arg_keys[4], (CANDS,), 0, ITEMS), jax.random.fold_in(arg_keys[4], 1), 0, ITEMS - 1).astype(jnp.int32)
    theta = bell_draw(arg_keys[5], (F,), F ** -0.5, 0.046875, ((0, 8),), jnp.float32)
    return {"shared_rows": shared_rows, "event_counts": event_counts, "ridge": ridge, "items": items, "cand_ids": cand_ids, "theta": theta}


def reference(shared_rows, event_counts, ridge, items, cand_ids, theta):
    slot = jnp.arange(EVENTS, dtype=jnp.int32)
    live = slot % EV_DEV < event_counts[slot // EV_DEV]
    masked = jnp.where(live[:, None], shared_rows, jnp.float32(0.0))
    gram = lax.dot_general(masked, masked, (((0,), (0,)), ((), ())), precision=lax.Precision.HIGHEST, preferred_element_type=jnp.float32)
    index = jnp.arange(F, dtype=jnp.int32)
    gram = gram.at[index, index].add(ridge)
    cands = items[cand_ids]
    image = lax.dot_general(cands, gram, (((1,), (1,)), ((), ())), precision=lax.Precision.HIGHEST, preferred_element_type=jnp.float32)
    quad = lax.optimization_barrier(jnp.sum(cands * image, axis=1))
    linear = jnp.dot(cands, theta, precision=lax.Precision.HIGHEST, preferred_element_type=jnp.float32)
    return (gram, linear + jnp.sqrt(quad / F))
```

```python
import jax
import jax.numpy as jnp
from jax import lax
from jax.sharding import PartitionSpec as P

F = 16384

highest = lax.Precision.HIGHEST


def body(shared_rows, event_counts, ridge, items, cand_ids, theta):
    n_row = lax.axis_size("row")
    n_col = lax.axis_size("col")
    ratio = n_row // n_col
    row_pos = lax.axis_index("row")
    col_pos = lax.axis_index("col")
    ev_slots, width_col = shared_rows.shape
    width_row = width_col // ratio
    slot = lax.iota(jnp.int32, ev_slots)
    masked = jnp.where((slot < event_counts[row_pos])[:, None], shared_rows, jnp.float32(0.0))

    col_all = lax.all_gather(masked, "row", axis=0, tiled=True)

    halves = masked.reshape(ev_slots, ratio, width_row)
    received = []
    for t in range(ratio):
        perm = []
        for s in range(n_row):
            for c in range(n_col):
                b = (s % ratio) ^ t
                perm.append((s * n_col + c, (ratio * c + b) * n_col + s // ratio))
        piece = halves[:, (row_pos % ratio) ^ t, :]
        received.append(lax.ppermute(piece, ("row", "col"), perm))
    parity = row_pos % ratio
    ordered = [
        sum(jnp.where(parity ^ t == a, received[t], 0.0) for t in range(ratio))
        for a in range(ratio)
    ]
    row_block = jnp.concatenate(ordered, axis=0)
    row_all = lax.all_gather(row_block, "col", axis=0, tiled=True)

    contract = (((0,), (0,)), ((), ()))
    tile = lax.dot_general(
        row_all, col_all, contract, precision=highest, preferred_element_type=jnp.float32
    )
    rows_global = row_pos * width_row + lax.broadcasted_iota(jnp.int32, (width_row, width_col), 0)
    cols_global = col_pos * width_col + lax.broadcasted_iota(jnp.int32, (width_row, width_col), 1)
    tile = tile + jnp.where(rows_global == cols_global, ridge[None, :], jnp.float32(0.0))

    z_part = lax.dot_general(
        col_all, items, (((1,), (1,)), ((), ())), precision=highest,
        preferred_element_type=jnp.float32,
    )
    z = lax.psum_scatter(z_part, "col", scatter_dimension=0, tiled=True)
    q_ev = jnp.sum(z * z, axis=0)
    q_ridge = jnp.sum(ridge[None, :] * items * items, axis=1)
    lin = jnp.dot(items, theta, precision=highest, preferred_element_type=jnp.float32)
    tot = lax.psum(jnp.stack([q_ev + q_ridge, lin]), "col")
    item_scores = tot[1] + jnp.sqrt(tot[0] / F)
    all_scores = lax.all_gather(item_scores, "row", axis=0, tiled=True)
    scores = all_scores[cand_ids]
    return (tile, scores)


def solution(mesh):
    return jax.shard_map(
        body,
        mesh=mesh,
        in_specs=(P("row", "col"), P(), P("col"), P("row", "col"), P(), P("col")),
        out_specs=(P("row", "col"), P()),
        check_vma=False,
    )
```

```python
import jax
import jax.numpy as jnp
from jax import lax
from jax.sharding import PartitionSpec as P

F = 16384

highest = lax.Precision.HIGHEST
high = lax.Precision.HIGH


def body(shared_rows, event_counts, ridge, items, cand_ids, theta):
    n_row = lax.axis_size("row")
    n_col = lax.axis_size("col")
    ratio = n_row // n_col
    row_pos = lax.axis_index("row")
    col_pos = lax.axis_index("col")
    ev_slots, width_col = shared_rows.shape
    width_row = width_col // ratio
    slot = lax.iota(jnp.int32, ev_slots)
    masked = jnp.where((slot < event_counts[row_pos])[:, None], shared_rows, jnp.float32(0.0))

    col_all = lax.all_gather(masked, "row", axis=0, tiled=True)

    halves = masked.reshape(ev_slots, ratio, width_row)
    received = []
    for t in range(ratio):
        perm = []
        for s in range(n_row):
            for c in range(n_col):
                b = (s % ratio) ^ t
                perm.append((s * n_col + c, (ratio * c + b) * n_col + s // ratio))
        piece = halves[:, (row_pos % ratio) ^ t, :]
        received.append(lax.ppermute(piece, ("row", "col"), perm))
    parity = row_pos % ratio
    ordered = [
        sum(jnp.where(parity ^ t == a, received[t], 0.0) for t in range(ratio))
        for a in range(ratio)
    ]
    row_block = jnp.concatenate(ordered, axis=0)

    n_y = n_col // 2
    ring = [y * 2 for y in range(n_y)] + [y * 2 + 1 for y in reversed(range(n_y))]
    where_in_ring = [ring.index(c) for c in range(n_col)]
    forward = [(ring[p], ring[(p + 1) % n_col]) for p in range(n_col)]
    backward = [(ring[p], ring[(p - 1) % n_col]) for p in range(n_col)]
    block_rows = row_block.shape[0]
    half_rows = block_rows // 2
    ring_tab = jnp.array(ring, jnp.int32)
    me = jnp.array(where_in_ring, jnp.int32)[col_pos]
    row_all = jnp.zeros((n_col * block_rows, width_row), jnp.float32)
    ahead, behind = row_block[:half_rows], row_block[half_rows:]
    row_all = lax.dynamic_update_slice_in_dim(row_all, ahead, col_pos * block_rows, 0)
    row_all = lax.dynamic_update_slice_in_dim(row_all, behind, col_pos * block_rows + half_rows, 0)
    for k in range(1, n_col):
        ahead = lax.ppermute(ahead, "col", forward)
        behind = lax.ppermute(behind, "col", backward)
        from_ahead = ring_tab[(me - k) % n_col]
        from_behind = ring_tab[(me + k) % n_col]
        row_all = lax.dynamic_update_slice_in_dim(row_all, ahead, from_ahead * block_rows, 0)
        row_all = lax.dynamic_update_slice_in_dim(
            row_all, behind, from_behind * block_rows + half_rows, 0
        )

    contract = (((0,), (0,)), ((), ()))
    tile = lax.dot_general(
        row_all, col_all, contract, precision=high, preferred_element_type=jnp.float32
    )
    rows_global = row_pos * width_row + lax.broadcasted_iota(jnp.int32, (width_row, width_col), 0)
    cols_global = col_pos * width_col + lax.broadcasted_iota(jnp.int32, (width_row, width_col), 1)
    tile = tile + jnp.where(rows_global == cols_global, ridge[None, :], jnp.float32(0.0))

    z_part = lax.dot_general(
        col_all, items, (((1,), (1,)), ((), ())), precision=high,
        preferred_element_type=jnp.float32,
    )
    z = lax.psum_scatter(z_part, "col", scatter_dimension=0, tiled=True)
    q_ev = jnp.sum(z * z, axis=0)
    q_ridge = jnp.sum(ridge[None, :] * items * items, axis=1)
    lin = jnp.dot(items, theta, precision=highest, preferred_element_type=jnp.float32)
    items_dev = items.shape[0]
    mine = jnp.stack([q_ev + q_ridge, lin])
    slot_of = lax.broadcasted_iota(jnp.int32, (2, n_row * items_dev), 1) // items_dev
    spread_out = jnp.where(slot_of == row_pos, jnp.tile(mine, (1, n_row)), jnp.float32(0.0))
    tot = lax.psum(spread_out, ("row", "col"))
    all_scores = tot[1] + jnp.sqrt(tot[0] / F)
    scores = all_scores[cand_ids]
    return (tile, scores)


def solution(mesh):
    return jax.shard_map(
        body,
        mesh=mesh,
        in_specs=(P("row", "col"), P(), P("col"), P("row", "col"), P(), P("col")),
        out_specs=(P("row", "col"), P()),
        check_vma=False,
    )
```

```python
import jax
import jax.numpy as jnp
from jax import lax
from jax.sharding import PartitionSpec as P

F = 16384

highest = lax.Precision.HIGHEST
high = lax.Precision.HIGH


def body(shared_rows, event_counts, ridge, items, cand_ids, theta):
    n_row = lax.axis_size("row")
    n_col = lax.axis_size("col")
    ratio = n_row // n_col
    row_pos = lax.axis_index("row")
    col_pos = lax.axis_index("col")
    ev_slots, width_col = shared_rows.shape
    width_row = width_col // ratio
    slot = lax.iota(jnp.int32, ev_slots)
    masked = jnp.where((slot < event_counts[row_pos])[:, None], shared_rows, jnp.float32(0.0))

    col_all = lax.all_gather(masked, "row", axis=0, tiled=True)

    halves = masked.reshape(ev_slots, ratio, width_row)
    received = []
    for t in range(ratio):
        perm = []
        for s in range(n_row):
            for c in range(n_col):
                b = (s % ratio) ^ t
                perm.append((s * n_col + c, (ratio * c + b) * n_col + s // ratio))
        piece = halves[:, (row_pos % ratio) ^ t, :]
        received.append(lax.ppermute(piece, ("row", "col"), perm))
    parity = row_pos % ratio
    ordered = [
        sum(jnp.where(parity ^ t == a, received[t], 0.0) for t in range(ratio))
        for a in range(ratio)
    ]
    row_block = jnp.concatenate(ordered, axis=0)

    n_y = n_col // 2
    ring = [y * 2 for y in range(n_y)] + [y * 2 + 1 for y in reversed(range(n_y))]
    where_in_ring = [ring.index(c) for c in range(n_col)]
    forward = [(ring[p], ring[(p + 1) % n_col]) for p in range(n_col)]
    backward = [(ring[p], ring[(p - 1) % n_col]) for p in range(n_col)]
    block_rows = row_block.shape[0]
    half_rows = block_rows // 2
    ring_tab = jnp.array(ring, jnp.int32)
    me = jnp.array(where_in_ring, jnp.int32)[col_pos]
    row_all = jnp.zeros((n_col * block_rows, width_row), jnp.float32)
    ahead, behind = row_block[:half_rows], row_block[half_rows:]
    row_all = lax.dynamic_update_slice_in_dim(row_all, ahead, col_pos * block_rows, 0)
    row_all = lax.dynamic_update_slice_in_dim(row_all, behind, col_pos * block_rows + half_rows, 0)
    for k in range(1, n_col):
        ahead = lax.ppermute(ahead, "col", forward)
        behind = lax.ppermute(behind, "col", backward)
        from_ahead = ring_tab[(me - k) % n_col]
        from_behind = ring_tab[(me + k) % n_col]
        row_all = lax.dynamic_update_slice_in_dim(row_all, ahead, from_ahead * block_rows, 0)
        row_all = lax.dynamic_update_slice_in_dim(
            row_all, behind, from_behind * block_rows + half_rows, 0
        )

    contract = (((0,), (0,)), ((), ()))
    tile = lax.dot_general(
        row_all, col_all, contract, precision=high, preferred_element_type=jnp.float32
    )
    rows_global = row_pos * width_row + lax.broadcasted_iota(jnp.int32, (width_row, width_col), 0)
    cols_global = col_pos * width_col + lax.broadcasted_iota(jnp.int32, (width_row, width_col), 1)
    tile = tile + jnp.where(rows_global == cols_global, ridge[None, :], jnp.float32(0.0))

    z_part = lax.dot_general(
        col_all, items, (((1,), (1,)), ((), ())), precision=high,
        preferred_element_type=jnp.float32,
    )
    q_ridge = jnp.sum(ridge[None, :] * items * items, axis=1)
    lin = jnp.dot(items, theta, precision=highest, preferred_element_type=jnp.float32)
    packed = jnp.concatenate([z_part, q_ridge[None, :], lin[None, :]], axis=0)
    step = n_col // 2
    while step >= 1:
        pairs = [(c, c ^ step) for c in range(n_col)]
        packed = packed + lax.ppermute(packed, "col", pairs)
        step //= 2
    ev_all = z_part.shape[0]
    z = packed[:ev_all]
    quad = jnp.sum(z * z, axis=0) + packed[ev_all]
    item_scores = packed[ev_all + 1] + jnp.sqrt(quad / F)
    items_dev = items.shape[0]
    held = item_scores
    step = 1
    while step < n_row:
        pairs = [(r, r ^ step) for r in range(n_row)]
        other = lax.ppermute(held, "row", pairs)
        low = (row_pos & step) == 0
        held = jnp.where(low, jnp.concatenate([held, other]), jnp.concatenate([other, held]))
        step *= 2
    scores = held[cand_ids]
    return (tile, scores)


def solution(mesh):
    return jax.shard_map(
        body,
        mesh=mesh,
        in_specs=(P("row", "col"), P(), P("col"), P("row", "col"), P(), P("col")),
        out_specs=(P("row", "col"), P()),
        check_vma=False,
    )
```

```python
import jax
import jax.numpy as jnp
from jax import lax
from jax.sharding import PartitionSpec as P

F = 16384

highest = lax.Precision.HIGHEST
high = lax.Precision.HIGH


def body(shared_rows, event_counts, ridge, items, cand_ids, theta):
    n_row = lax.axis_size("row")
    n_col = lax.axis_size("col")
    ratio = n_row // n_col
    row_pos = lax.axis_index("row")
    col_pos = lax.axis_index("col")
    ev_slots, width_col = shared_rows.shape
    width_row = width_col // ratio
    slot = lax.iota(jnp.int32, ev_slots)
    masked = jnp.where((slot < event_counts[row_pos])[:, None], shared_rows, jnp.float32(0.0))

    col_all = lax.all_gather(masked, "row", axis=0, tiled=True)

    halves = masked.reshape(ev_slots, ratio, width_row)
    received = []
    for t in range(ratio):
        perm = []
        for s in range(n_row):
            for c in range(n_col):
                b = (s % ratio) ^ t
                perm.append((s * n_col + c, (ratio * c + b) * n_col + s // ratio))
        piece = halves[:, (row_pos % ratio) ^ t, :]
        received.append(lax.ppermute(piece, ("row", "col"), perm))
    parity = row_pos % ratio
    ordered = [
        sum(jnp.where(parity ^ t == a, received[t], 0.0) for t in range(ratio))
        for a in range(ratio)
    ]
    row_block = jnp.concatenate(ordered, axis=0)

    block_rows = row_block.shape[0]
    row_all = jnp.zeros((n_col * block_rows, width_row), jnp.float32)
    row_all = lax.dynamic_update_slice_in_dim(row_all, row_block, col_pos * block_rows, 0)
    for k in range(1, n_col):
        pairs = [(c, c ^ k) for c in range(n_col)]
        got = lax.ppermute(row_block, "col", pairs)
        row_all = lax.dynamic_update_slice_in_dim(row_all, got, (col_pos ^ k) * block_rows, 0)

    col_all, row_all = lax.optimization_barrier((col_all, row_all))
    contract = (((0,), (0,)), ((), ()))
    tile = lax.dot_general(
        row_all, col_all, contract, precision=high, preferred_element_type=jnp.float32
    )
    rows_global = row_pos * width_row + lax.broadcasted_iota(jnp.int32, (width_row, width_col), 0)
    cols_global = col_pos * width_col + lax.broadcasted_iota(jnp.int32, (width_row, width_col), 1)
    tile = tile + jnp.where(rows_global == cols_global, ridge[None, :], jnp.float32(0.0))

    z_part = lax.dot_general(
        col_all, items, (((1,), (1,)), ((), ())), precision=high,
        preferred_element_type=jnp.float32,
    )
    q_ridge = jnp.sum(ridge[None, :] * items * items, axis=1)
    lin = jnp.dot(items, theta, precision=highest, preferred_element_type=jnp.float32)
    packed = jnp.concatenate([z_part, q_ridge[None, :], lin[None, :]], axis=0)
    step = n_col // 2
    while step >= 1:
        pairs = [(c, c ^ step) for c in range(n_col)]
        packed = packed + lax.ppermute(packed, "col", pairs)
        step //= 2
    ev_all = z_part.shape[0]
    z = packed[:ev_all]
    quad = jnp.sum(z * z, axis=0) + packed[ev_all]
    item_scores = packed[ev_all + 1] + jnp.sqrt(quad / F)
    items_dev = items.shape[0]
    held = item_scores
    step = 1
    while step < n_row:
        pairs = [(r, r ^ step) for r in range(n_row)]
        other = lax.ppermute(held, "row", pairs)
        low = (row_pos & step) == 0
        held = jnp.where(low, jnp.concatenate([held, other]), jnp.concatenate([other, held]))
        step *= 2
    scores = held[cand_ids]
    return (tile, scores)


def solution(mesh):
    return jax.shard_map(
        body,
        mesh=mesh,
        in_specs=(P("row", "col"), P(), P("col"), P("row", "col"), P(), P("col")),
        out_specs=(P("row", "col"), P()),
        check_vma=False,
    )
```

```python
import jax
import jax.numpy as jnp
from jax import lax
from jax.sharding import Mesh
from jax.sharding import PartitionSpec as P

F = 16384

highest = lax.Precision.HIGHEST
high = lax.Precision.HIGH
ROW = ("chip", "core")


def body(shared_rows, event_counts, ridge, items, cand_ids, theta):
    n_chip = lax.axis_size("chip")
    n_core = lax.axis_size("core")
    n_row = n_chip * n_core
    n_col = lax.axis_size("col")
    ratio = n_row // n_col
    core = lax.axis_index("core")
    row_pos = lax.axis_index("chip") * n_core + core
    col_pos = lax.axis_index("col")
    ev_slots, width_col = shared_rows.shape
    width_row = width_col // ratio
    slot = lax.iota(jnp.int32, ev_slots)
    masked = jnp.where((slot < event_counts[row_pos])[:, None], shared_rows, jnp.float32(0.0))

    col_mine = lax.all_gather(masked, "chip", axis=0, tiled=True)

    halves = masked.reshape(ev_slots, ratio, width_row)
    received = []
    for t in range(ratio):
        perm = []
        for s in range(n_row):
            for c in range(n_col):
                b = (s % ratio) ^ t
                perm.append((s * n_col + c, (ratio * c + b) * n_col + s // ratio))
        piece = halves[:, (row_pos % ratio) ^ t, :]
        received.append(lax.ppermute(piece, ("chip", "core", "col"), perm))
    row_block = jnp.concatenate(received, axis=0)

    half = ev_slots * n_col
    pieces = [(col_pos, row_block)]
    for k in range(1, n_col):
        pairs = [(c, c ^ k) for c in range(n_col)]
        pieces.append((col_pos ^ k, lax.ppermute(row_block, "col", pairs)))
    row_all = jnp.zeros((2 * half, width_row), jnp.float32)
    for src, got in pieces:
        row_all = lax.dynamic_update_slice_in_dim(row_all, got[:ev_slots], src * ev_slots, 0)
        row_all = lax.dynamic_update_slice_in_dim(
            row_all, got[ev_slots:], half + src * ev_slots, 0
        )

    col_mine, row_all = lax.optimization_barrier((col_mine, row_all))
    col_other = lax.ppermute(col_mine, "core", [(0, 1), (1, 0)])

    contract = (((0,), (0,)), ((), ()))
    tile = lax.dot_general(
        row_all[:half], col_mine, contract, precision=high, preferred_element_type=jnp.float32
    )
    tile = tile + lax.dot_general(
        row_all[half:], col_other, contract, precision=high, preferred_element_type=jnp.float32
    )
    rows_global = row_pos * width_row + lax.broadcasted_iota(jnp.int32, (width_row, width_col), 0)
    cols_global = col_pos * width_col + lax.broadcasted_iota(jnp.int32, (width_row, width_col), 1)
    tile = tile + jnp.where(rows_global == cols_global, ridge[None, :], jnp.float32(0.0))

    across = (((1,), (1,)), ((), ()))
    z_part = jnp.concatenate([
        lax.dot_general(col_mine, items, across, precision=high, preferred_element_type=jnp.float32),
        lax.dot_general(col_other, items, across, precision=high, preferred_element_type=jnp.float32),
    ], axis=0)
    q_ridge = jnp.sum(ridge[None, :] * items * items, axis=1)
    lin = jnp.dot(items, theta, precision=highest, preferred_element_type=jnp.float32)
    packed = jnp.concatenate([z_part, q_ridge[None, :], lin[None, :]], axis=0)
    step = n_col // 2
    while step >= 1:
        pairs = [(c, c ^ step) for c in range(n_col)]
        packed = packed + lax.ppermute(packed, "col", pairs)
        step //= 2
    ev_all = z_part.shape[0]
    z = packed[:ev_all]
    quad = jnp.sum(z * z, axis=0) + packed[ev_all]
    item_scores = packed[ev_all + 1] + jnp.sqrt(quad / F)
    held = item_scores
    step = 1
    while step < n_row:
        pairs = [(r, r ^ step) for r in range(n_row)]
        other = lax.ppermute(held, ROW, pairs)
        low = (row_pos & step) == 0
        held = jnp.where(low, jnp.concatenate([held, other]), jnp.concatenate([other, held]))
        step *= 2
    scores = held[cand_ids]
    return (tile, scores)


def solution(mesh):
    n_row = mesh.shape["row"]
    n_col = mesh.shape["col"]
    inner = Mesh(mesh.devices.reshape(n_row // 2, 2, n_col), ("chip", "core", "col"))
    return jax.shard_map(
        body,
        mesh=inner,
        in_specs=(P(ROW, "col"), P(), P("col"), P(ROW, "col"), P(), P("col")),
        out_specs=(P(ROW, "col"), P()),
        check_vma=False,
    )
```

```python
import jax
import jax.numpy as jnp
from jax import lax
from jax.sharding import PartitionSpec as P

F = 16384

highest = lax.Precision.HIGHEST
high = lax.Precision.HIGH


def body(shared_rows, event_counts, ridge, items, cand_ids, theta):
    n_row = lax.axis_size("row")
    n_col = lax.axis_size("col")
    ratio = n_row // n_col
    row_pos = lax.axis_index("row")
    col_pos = lax.axis_index("col")
    ev_slots, width_col = shared_rows.shape
    width_row = width_col // ratio
    slot = lax.iota(jnp.int32, ev_slots)
    masked = jnp.where((slot < event_counts[row_pos])[:, None], shared_rows, jnp.float32(0.0))

    col_all = lax.all_gather(masked, "row", axis=0, tiled=True)

    halves = masked.reshape(ev_slots, ratio, width_row)
    received = []
    for t in range(ratio):
        perm = []
        for s in range(n_row):
            for c in range(n_col):
                b = (s % ratio) ^ t
                perm.append((s * n_col + c, (ratio * c + b) * n_col + s // ratio))
        piece = halves[:, (row_pos % ratio) ^ t, :]
        received.append(lax.ppermute(piece, ("row", "col"), perm))
    parity = row_pos % ratio
    ordered = [
        sum(jnp.where(parity ^ t == a, received[t], 0.0) for t in range(ratio))
        for a in range(ratio)
    ]
    n_y = n_col // 2
    ring = [y * 2 for y in range(n_y)] + [y * 2 + 1 for y in reversed(range(n_y))]
    where_in_ring = [ring.index(c) for c in range(n_col)]
    forward = [(ring[p], ring[(p + 1) % n_col]) for p in range(n_col)]
    backward = [(ring[p], ring[(p - 1) % n_col]) for p in range(n_col)]
    half_rows = ev_slots // 2
    ring_tab = jnp.array(ring, jnp.int32)
    me = jnp.array(where_in_ring, jnp.int32)[col_pos]
    row_even = jnp.zeros((n_col * ev_slots, width_row), jnp.float32)
    ahead, behind = ordered[0][:half_rows], ordered[0][half_rows:]
    row_even = lax.dynamic_update_slice_in_dim(row_even, ahead, col_pos * ev_slots, 0)
    row_even = lax.dynamic_update_slice_in_dim(row_even, behind, col_pos * ev_slots + half_rows, 0)
    for k in range(1, n_col):
        ahead = lax.ppermute(ahead, "col", forward)
        behind = lax.ppermute(behind, "col", backward)
        from_ahead = ring_tab[(me - k) % n_col]
        from_behind = ring_tab[(me + k) % n_col]
        row_even = lax.dynamic_update_slice_in_dim(row_even, ahead, from_ahead * ev_slots, 0)
        row_even = lax.dynamic_update_slice_in_dim(
            row_even, behind, from_behind * ev_slots + half_rows, 0
        )
    row_odd = lax.all_gather(ordered[1], "col", axis=0, tiled=True)

    by_shard = col_all.reshape(n_col, ratio, ev_slots, width_col)
    contract = (((0,), (0,)), ((), ()))
    tile = lax.dot_general(
        row_even, by_shard[:, 0].reshape(n_col * ev_slots, width_col), contract,
        precision=high, preferred_element_type=jnp.float32,
    )
    tile = tile + lax.dot_general(
        row_odd, by_shard[:, 1].reshape(n_col * ev_slots, width_col), contract,
        precision=high, preferred_element_type=jnp.float32,
    )
    rows_global = row_pos * width_row + lax.broadcasted_iota(jnp.int32, (width_row, width_col), 0)
    cols_global = col_pos * width_col + lax.broadcasted_iota(jnp.int32, (width_row, width_col), 1)
    tile = tile + jnp.where(rows_global == cols_global, ridge[None, :], jnp.float32(0.0))

    z_part = lax.dot_general(
        col_all, items, (((1,), (1,)), ((), ())), precision=high,
        preferred_element_type=jnp.float32,
    )
    q_ridge = jnp.sum(ridge[None, :] * items * items, axis=1)
    lin = jnp.dot(items, theta, precision=highest, preferred_element_type=jnp.float32)
    packed = jnp.concatenate([z_part, q_ridge[None, :], lin[None, :]], axis=0)
    step = n_col // 2
    while step >= 1:
        pairs = [(c, c ^ step) for c in range(n_col)]
        packed = packed + lax.ppermute(packed, "col", pairs)
        step //= 2
    ev_all = z_part.shape[0]
    z = packed[:ev_all]
    quad = jnp.sum(z * z, axis=0) + packed[ev_all]
    item_scores = packed[ev_all + 1] + jnp.sqrt(quad / F)
    items_dev = items.shape[0]
    held = item_scores
    step = 1
    while step < n_row:
        pairs = [(r, r ^ step) for r in range(n_row)]
        other = lax.ppermute(held, "row", pairs)
        low = (row_pos & step) == 0
        held = jnp.where(low, jnp.concatenate([held, other]), jnp.concatenate([other, held]))
        step *= 2
    scores = held[cand_ids]
    return (tile, scores)


def solution(mesh):
    return jax.shard_map(
        body,
        mesh=mesh,
        in_specs=(P("row", "col"), P(), P("col"), P("row", "col"), P(), P("col")),
        out_specs=(P("row", "col"), P()),
        check_vma=False,
    )
```

```python
import jax
import jax.numpy as jnp
from jax import lax
from jax.sharding import PartitionSpec as P

F = 16384

highest = lax.Precision.HIGHEST
high = lax.Precision.HIGH


def body(shared_rows, event_counts, ridge, items, cand_ids, theta):
    n_row = lax.axis_size("row")
    n_col = lax.axis_size("col")
    ratio = n_row // n_col
    row_pos = lax.axis_index("row")
    col_pos = lax.axis_index("col")
    ev_slots, width_col = shared_rows.shape
    width_row = width_col // ratio
    slot = lax.iota(jnp.int32, ev_slots)
    masked = jnp.where((slot < event_counts[row_pos])[:, None], shared_rows, jnp.float32(0.0))

    col_all = lax.all_gather(masked, "row", axis=0, tiled=True)

    halves = masked.reshape(ev_slots, ratio, width_row)
    received = []
    for t in range(ratio):
        perm = []
        for s in range(n_row):
            for c in range(n_col):
                b = (s % ratio) ^ t
                perm.append((s * n_col + c, (ratio * c + b) * n_col + s // ratio))
        piece = halves[:, (row_pos % ratio) ^ t, :]
        received.append(lax.ppermute(piece, ("row", "col"), perm))
    parity = row_pos % ratio
    ordered = [
        sum(jnp.where(parity ^ t == a, received[t], 0.0) for t in range(ratio))
        for a in range(ratio)
    ]
    row_block = jnp.concatenate(ordered, axis=0)

    n_y = n_col // 2
    ring = [y * 2 for y in range(n_y)] + [y * 2 + 1 for y in reversed(range(n_y))]
    where_in_ring = [ring.index(c) for c in range(n_col)]
    forward = [(ring[p], ring[(p + 1) % n_col]) for p in range(n_col)]
    backward = [(ring[p], ring[(p - 1) % n_col]) for p in range(n_col)]
    block_rows = row_block.shape[0]
    half_rows = block_rows // 2
    ring_tab = jnp.array(ring, jnp.int32)
    me = jnp.array(where_in_ring, jnp.int32)[col_pos]
    ahead, behind = row_block[:half_rows], row_block[half_rows:]
    pieces = [(ahead, col_pos * block_rows), (behind, col_pos * block_rows + half_rows)]
    contract = (((0,), (0,)), ((), ()))
    early = 2 * (n_col // 2 + 1)

    def part_product(part):
        rows = jnp.concatenate([p for p, _ in part], axis=0)
        cols = jnp.concatenate(
            [lax.dynamic_slice_in_dim(col_all, off, half_rows, 0) for _, off in part], axis=0
        )
        return lax.dot_general(
            rows, cols, contract, precision=high, preferred_element_type=jnp.float32
        )

    tile = None
    for k in range(1, n_col):
        ahead = lax.ppermute(ahead, "col", forward)
        behind = lax.ppermute(behind, "col", backward)
        pieces.append((ahead, ring_tab[(me - k) % n_col] * block_rows))
        pieces.append((behind, ring_tab[(me + k) % n_col] * block_rows + half_rows))
        if k == n_col // 2:
            col_all, ahead, behind = lax.optimization_barrier((col_all, ahead, behind))
        if k == n_col // 2 + 1:
            tile = part_product(pieces[:early])
            tile, col_all, ahead, behind = lax.optimization_barrier((tile, col_all, ahead, behind))
    tile = tile + part_product(pieces[early:])
    rows_global = row_pos * width_row + lax.broadcasted_iota(jnp.int32, (width_row, width_col), 0)
    cols_global = col_pos * width_col + lax.broadcasted_iota(jnp.int32, (width_row, width_col), 1)
    tile = tile + jnp.where(rows_global == cols_global, ridge[None, :], jnp.float32(0.0))

    z_part = lax.dot_general(
        col_all, items, (((1,), (1,)), ((), ())), precision=high,
        preferred_element_type=jnp.float32,
    )
    q_ridge = jnp.sum(ridge[None, :] * items * items, axis=1)
    lin = jnp.dot(items, theta, precision=highest, preferred_element_type=jnp.float32)
    packed = jnp.concatenate([z_part, q_ridge[None, :], lin[None, :]], axis=0)
    step = n_col // 2
    while step >= 1:
        pairs = [(c, c ^ step) for c in range(n_col)]
        packed = packed + lax.ppermute(packed, "col", pairs)
        step //= 2
    ev_all = z_part.shape[0]
    z = packed[:ev_all]
    quad = jnp.sum(z * z, axis=0) + packed[ev_all]
    item_scores = packed[ev_all + 1] + jnp.sqrt(quad / F)
    items_dev = items.shape[0]
    held = item_scores
    step = 1
    while step < n_row:
        pairs = [(r, r ^ step) for r in range(n_row)]
        other = lax.ppermute(held, "row", pairs)
        low = (row_pos & step) == 0
        held = jnp.where(low, jnp.concatenate([held, other]), jnp.concatenate([other, held]))
        step *= 2
    scores = held[cand_ids]
    return (tile, scores)


def solution(mesh):
    return jax.shard_map(
        body,
        mesh=mesh,
        in_specs=(P("row", "col"), P(), P("col"), P("row", "col"), P(), P("col")),
        out_specs=(P("row", "col"), P()),
        check_vma=False,
    )
```

```python
import jax
import jax.numpy as jnp
from jax import lax
from jax.sharding import Mesh
from jax.sharding import PartitionSpec as P

F = 16384

highest = lax.Precision.HIGHEST
high = lax.Precision.HIGH
ROW = ("zl", "x", "core")
COL = ("y", "zh")


def body(shared_rows, event_counts, ridge, items, cand_ids, theta):
    n_row = lax.axis_size("zl") * lax.axis_size("x") * lax.axis_size("core")
    n_col = lax.axis_size("y") * lax.axis_size("zh")
    ratio = n_row // n_col
    row_pos = (lax.axis_index("zl") * lax.axis_size("x") + lax.axis_index("x")) * lax.axis_size(
        "core"
    ) + lax.axis_index("core")
    col_pos = lax.axis_index("y") * lax.axis_size("zh") + lax.axis_index("zh")
    ev_slots, width_col = shared_rows.shape
    width_row = width_col // ratio
    slot = lax.iota(jnp.int32, ev_slots)
    masked = jnp.where((slot < event_counts[row_pos])[:, None], shared_rows, jnp.float32(0.0))

    col_all = masked
    for name in reversed(ROW):
        col_all = lax.all_gather(col_all, name, axis=0, tiled=True)

    halves = masked.reshape(ev_slots, ratio, width_row)
    received = []
    for t in range(ratio):
        perm = []
        for s in range(n_row):
            for c in range(n_col):
                b = (s % ratio) ^ t
                perm.append((s * n_col + c, (ratio * c + b) * n_col + s // ratio))
        piece = halves[:, (row_pos % ratio) ^ t, :]
        received.append(lax.ppermute(piece, ROW + COL, perm))
    parity = row_pos % ratio
    ordered = [
        sum(jnp.where(parity ^ t == a, received[t], 0.0) for t in range(ratio))
        for a in range(ratio)
    ]
    row_block = jnp.concatenate(ordered, axis=0)

    row_all = row_block
    for name in reversed(COL):
        row_all = lax.all_gather(row_all, name, axis=0, tiled=True)

    contract = (((0,), (0,)), ((), ()))
    tile = lax.dot_general(
        row_all, col_all, contract, precision=high, preferred_element_type=jnp.float32
    )
    rows_global = row_pos * width_row + lax.broadcasted_iota(jnp.int32, (width_row, width_col), 0)
    cols_global = col_pos * width_col + lax.broadcasted_iota(jnp.int32, (width_row, width_col), 1)
    tile = tile + jnp.where(rows_global == cols_global, ridge[None, :], jnp.float32(0.0))

    z_part = lax.dot_general(
        col_all, items, (((1,), (1,)), ((), ())), precision=high,
        preferred_element_type=jnp.float32,
    )
    q_ridge = jnp.sum(ridge[None, :] * items * items, axis=1)
    lin = jnp.dot(items, theta, precision=highest, preferred_element_type=jnp.float32)
    packed = jnp.concatenate([z_part, q_ridge[None, :], lin[None, :]], axis=0)
    step = n_col // 2
    while step >= 1:
        pairs = [(c, c ^ step) for c in range(n_col)]
        packed = packed + lax.ppermute(packed, COL, pairs)
        step //= 2
    ev_all = z_part.shape[0]
    z = packed[:ev_all]
    quad = jnp.sum(z * z, axis=0) + packed[ev_all]
    item_scores = packed[ev_all + 1] + jnp.sqrt(quad / F)
    items_dev = items.shape[0]
    held = item_scores
    step = 1
    while step < n_row:
        pairs = [(r, r ^ step) for r in range(n_row)]
        other = lax.ppermute(held, ROW, pairs)
        low = (row_pos & step) == 0
        held = jnp.where(low, jnp.concatenate([held, other]), jnp.concatenate([other, held]))
        step *= 2
    scores = held[cand_ids]
    return (tile, scores)


def solution(mesh):
    n_row = mesh.shape["row"]
    n_col = mesh.shape["col"]
    inner = Mesh(mesh.devices.reshape(2, n_row // 4, 2, n_col // 2, 2), ROW + COL)
    return jax.shard_map(
        body,
        mesh=inner,
        in_specs=(P(ROW, COL), P(), P(COL), P(ROW, COL), P(), P(COL)),
        out_specs=(P(ROW, COL), P()),
        check_vma=False,
    )
```

```python
import jax
import jax.numpy as jnp
from jax import lax
from jax.sharding import PartitionSpec as P

F = 16384

highest = lax.Precision.HIGHEST
high = lax.Precision.HIGH


def body(shared_rows, event_counts, ridge, items, cand_ids, theta):
    n_row = lax.axis_size("row")
    n_col = lax.axis_size("col")
    ratio = n_row // n_col
    row_pos = lax.axis_index("row")
    col_pos = lax.axis_index("col")
    ev_slots, width_col = shared_rows.shape
    width_row = width_col // ratio
    slot = lax.iota(jnp.int32, ev_slots)
    masked = jnp.where((slot < event_counts[row_pos])[:, None], shared_rows, jnp.float32(0.0))

    col_all = lax.all_gather(masked, "row", axis=0, tiled=True)

    halves = masked.reshape(ev_slots, ratio, width_row)
    received = []
    for t in range(ratio):
        perm = []
        for s in range(n_row):
            for c in range(n_col):
                b = (s % ratio) ^ t
                perm.append((s * n_col + c, (ratio * c + b) * n_col + s // ratio))
        piece = halves[:, (row_pos % ratio) ^ t, :]
        received.append(lax.ppermute(piece, ("row", "col"), perm))
    parity = row_pos % ratio
    ordered = [
        sum(jnp.where(parity ^ t == a, received[t], 0.0) for t in range(ratio))
        for a in range(ratio)
    ]
    row_block = jnp.concatenate(ordered, axis=0)

    n_y = n_col // 2
    ring = [y * 2 for y in range(n_y)] + [y * 2 + 1 for y in reversed(range(n_y))]
    where_in_ring = [ring.index(c) for c in range(n_col)]
    forward = [(ring[p], ring[(p + 1) % n_col]) for p in range(n_col)]
    backward = [(ring[p], ring[(p - 1) % n_col]) for p in range(n_col)]
    block_rows = row_block.shape[0]
    ring_tab = jnp.array(ring, jnp.int32)
    me = jnp.array(where_in_ring, jnp.int32)[col_pos]
    row_all = jnp.zeros((n_col * block_rows, width_row), jnp.float32)
    row_all = lax.dynamic_update_slice_in_dim(row_all, row_block, col_pos * block_rows, 0)
    ahead = behind = row_block
    for k in range(1, n_col // 2 + 1):
        ahead = lax.ppermute(ahead, "col", forward)
        row_all = lax.dynamic_update_slice_in_dim(
            row_all, ahead, ring_tab[(me - k) % n_col] * block_rows, 0
        )
        if k < n_col // 2:
            behind = lax.ppermute(behind, "col", backward)
            row_all = lax.dynamic_update_slice_in_dim(
                row_all, behind, ring_tab[(me + k) % n_col] * block_rows, 0
            )

    col_all, row_all = lax.optimization_barrier((col_all, row_all))
    contract = (((0,), (0,)), ((), ()))
    def rows_of_tile(lo, hi):
        return lax.dot_general(
            row_all[:, lo:hi], col_all, contract, precision=high,
            preferred_element_type=jnp.float32,
        )

    n_parts = 2
    part_rows = width_row // n_parts
    parts = []
    z_part = lax.dot_general(
        col_all, items, (((1,), (1,)), ((), ())), precision=high,
        preferred_element_type=jnp.float32,
    )
    q_ridge = jnp.sum(ridge[None, :] * items * items, axis=1)
    lin = jnp.dot(items, theta, precision=highest, preferred_element_type=jnp.float32)
    packed = jnp.concatenate([z_part, q_ridge[None, :], lin[None, :]], axis=0)
    step = n_col // 2
    while step >= 1:
        pairs = [(c, c ^ step) for c in range(n_col)]
        packed = packed + lax.ppermute(packed, "col", pairs)
        if len(parts) < n_parts:
            lo = len(parts) * part_rows
            part = rows_of_tile(lo, lo + part_rows)
            part, packed = lax.optimization_barrier((part, packed))
            parts.append(part)
        step //= 2
    tile = jnp.concatenate(parts, axis=0)
    rows_global = row_pos * width_row + lax.broadcasted_iota(jnp.int32, (width_row, width_col), 0)
    cols_global = col_pos * width_col + lax.broadcasted_iota(jnp.int32, (width_row, width_col), 1)
    tile = tile + jnp.where(rows_global == cols_global, ridge[None, :], jnp.float32(0.0))

    ev_all = z_part.shape[0]
    z = packed[:ev_all]
    quad = jnp.sum(z * z, axis=0) + packed[ev_all]
    item_scores = packed[ev_all + 1] + jnp.sqrt(quad / F)
    items_dev = items.shape[0]
    held = item_scores
    step = 1
    while step < n_row:
        pairs = [(r, r ^ step) for r in range(n_row)]
        other = lax.ppermute(held, "row", pairs)
        low = (row_pos & step) == 0
        held = jnp.where(low, jnp.concatenate([held, other]), jnp.concatenate([other, held]))
        step *= 2
    scores = held[cand_ids]
    return (tile, scores)


def solution(mesh):
    return jax.shard_map(
        body,
        mesh=mesh,
        in_specs=(P("row", "col"), P(), P("col"), P("row", "col"), P(), P("col")),
        out_specs=(P("row", "col"), P()),
        check_vma=False,
    )
```

```python
import jax
import jax.numpy as jnp
from jax import lax
from jax.sharding import PartitionSpec as P

F = 16384

highest = lax.Precision.HIGHEST
high = lax.Precision.HIGH


def body(shared_rows, event_counts, ridge, items, cand_ids, theta):
    n_row = lax.axis_size("row")
    n_col = lax.axis_size("col")
    ratio = n_row // n_col
    row_pos = lax.axis_index("row")
    col_pos = lax.axis_index("col")
    ev_slots, width_col = shared_rows.shape
    width_row = width_col // ratio
    slot = lax.iota(jnp.int32, ev_slots)
    masked = jnp.where((slot < event_counts[row_pos])[:, None], shared_rows, jnp.float32(0.0))

    col_all = lax.all_gather(masked, "row", axis=0, tiled=True)

    halves = masked.reshape(ev_slots, ratio, width_row)
    received = []
    for t in range(ratio):
        perm = []
        for s in range(n_row):
            for c in range(n_col):
                b = (s % ratio) ^ t
                perm.append((s * n_col + c, (ratio * c + b) * n_col + s // ratio))
        piece = halves[:, (row_pos % ratio) ^ t, :]
        received.append(lax.ppermute(piece, ("row", "col"), perm))
    parity = row_pos % ratio
    ordered = [
        sum(jnp.where(parity ^ t == a, received[t], 0.0) for t in range(ratio))
        for a in range(ratio)
    ]
    row_block = jnp.concatenate(ordered, axis=0)

    n_y = n_col // 2
    ring = [y * 2 for y in range(n_y)] + [y * 2 + 1 for y in reversed(range(n_y))]
    where_in_ring = [ring.index(c) for c in range(n_col)]
    forward = [(ring[p], ring[(p + 1) % n_col]) for p in range(n_col)]
    backward = [(ring[p], ring[(p - 1) % n_col]) for p in range(n_col)]
    block_rows = row_block.shape[0]
    ring_tab = jnp.array(ring, jnp.int32)
    me = jnp.array(where_in_ring, jnp.int32)[col_pos]
    row_all = jnp.zeros((n_col * block_rows, width_row), jnp.float32)
    row_all = lax.dynamic_update_slice_in_dim(row_all, row_block, col_pos * block_rows, 0)
    ahead = behind = row_block
    for k in range(1, n_col // 2 + 1):
        ahead = lax.ppermute(ahead, "col", forward)
        row_all = lax.dynamic_update_slice_in_dim(
            row_all, ahead, ring_tab[(me - k) % n_col] * block_rows, 0
        )
        if k < n_col // 2:
            behind = lax.ppermute(behind, "col", backward)
            row_all = lax.dynamic_update_slice_in_dim(
                row_all, behind, ring_tab[(me + k) % n_col] * block_rows, 0
            )

    col_all, row_all = lax.optimization_barrier((col_all, row_all))
    contract = (((0,), (0,)), ((), ()))
    tile = lax.dot_general(
        row_all, col_all, contract, precision=high, preferred_element_type=jnp.float32
    )
    tile, col_all = lax.optimization_barrier((tile, col_all))
    z_part = lax.dot_general(
        col_all, items, (((1,), (1,)), ((), ())), precision=high,
        preferred_element_type=jnp.float32,
    )
    q_ridge = jnp.sum(ridge[None, :] * items * items, axis=1)
    lin = jnp.dot(items, theta, precision=highest, preferred_element_type=jnp.float32)
    packed = jnp.concatenate([z_part, q_ridge[None, :], lin[None, :]], axis=0)
    step = n_col // 2
    while step >= 1:
        pairs = [(c, c ^ step) for c in range(n_col)]
        packed = packed + lax.ppermute(packed, "col", pairs)
        step //= 2
    rows_global = row_pos * width_row + lax.broadcasted_iota(jnp.int32, (width_row, width_col), 0)
    cols_global = col_pos * width_col + lax.broadcasted_iota(jnp.int32, (width_row, width_col), 1)
    tile = tile + jnp.where(rows_global == cols_global, ridge[None, :], jnp.float32(0.0))

    ev_all = z_part.shape[0]
    z = packed[:ev_all]
    quad = jnp.sum(z * z, axis=0) + packed[ev_all]
    item_scores = packed[ev_all + 1] + jnp.sqrt(quad / F)
    items_dev = items.shape[0]
    held = item_scores
    step = 1
    while step < n_row:
        pairs = [(r, r ^ step) for r in range(n_row)]
        other = lax.ppermute(held, "row", pairs)
        low = (row_pos & step) == 0
        held = jnp.where(low, jnp.concatenate([held, other]), jnp.concatenate([other, held]))
        step *= 2
    scores = held[cand_ids]
    return (tile, scores)


def solution(mesh):
    return jax.shard_map(
        body,
        mesh=mesh,
        in_specs=(P("row", "col"), P(), P("col"), P("row", "col"), P(), P("col")),
        out_specs=(P("row", "col"), P()),
        check_vma=False,
    )
```

```python
import jax
import jax.numpy as jnp
from jax import lax
from jax.sharding import PartitionSpec as P

F = 16384

highest = lax.Precision.HIGHEST
high = lax.Precision.HIGH


def body(shared_rows, event_counts, ridge, items, cand_ids, theta):
    n_row = lax.axis_size("row")
    n_col = lax.axis_size("col")
    ratio = n_row // n_col
    row_pos = lax.axis_index("row")
    col_pos = lax.axis_index("col")
    ev_slots, width_col = shared_rows.shape
    width_row = width_col // ratio
    slot = lax.iota(jnp.int32, ev_slots)
    masked = jnp.where((slot < event_counts[row_pos])[:, None], shared_rows, jnp.float32(0.0))

    col_all = lax.all_gather(masked, "row", axis=0, tiled=True)

    halves = masked.reshape(ev_slots, ratio, width_row)
    received = []
    for t in range(ratio):
        perm = []
        for s in range(n_row):
            for c in range(n_col):
                b = (s % ratio) ^ t
                perm.append((s * n_col + c, (ratio * c + b) * n_col + s // ratio))
        piece = halves[:, (row_pos % ratio) ^ t, :]
        received.append(lax.ppermute(piece, ("row", "col"), perm))
    parity = row_pos % ratio
    ordered = [
        sum(jnp.where(parity ^ t == a, received[t], 0.0) for t in range(ratio))
        for a in range(ratio)
    ]
    row_block = jnp.concatenate(ordered, axis=0)

    n_y = n_col // 2
    ring = [y * 2 for y in range(n_y)] + [y * 2 + 1 for y in reversed(range(n_y))]
    where_in_ring = [ring.index(c) for c in range(n_col)]
    forward = [(ring[p], ring[(p + 1) % n_col]) for p in range(n_col)]
    backward = [(ring[p], ring[(p - 1) % n_col]) for p in range(n_col)]
    block_rows = row_block.shape[0]
    ring_tab = jnp.array(ring, jnp.int32)
    me = jnp.array(where_in_ring, jnp.int32)[col_pos]
    row_all = jnp.zeros((n_col * block_rows, width_row), jnp.float32)
    row_all = lax.dynamic_update_slice_in_dim(row_all, row_block, col_pos * block_rows, 0)
    ahead = behind = row_block
    for k in range(1, n_col // 2 + 1):
        ahead = lax.ppermute(ahead, "col", forward)
        row_all = lax.dynamic_update_slice_in_dim(
            row_all, ahead, ring_tab[(me - k) % n_col] * block_rows, 0
        )
        if k < n_col // 2:
            behind = lax.ppermute(behind, "col", backward)
            row_all = lax.dynamic_update_slice_in_dim(
                row_all, behind, ring_tab[(me + k) % n_col] * block_rows, 0
            )

    col_all, row_all = lax.optimization_barrier((col_all, row_all))
    contract = (((0,), (0,)), ((), ()))
    tile = lax.dot_general(
        row_all, col_all, contract, precision=high, preferred_element_type=jnp.float32
    )
    z_part = lax.dot_general(
        col_all, items, (((1,), (1,)), ((), ())), precision=high,
        preferred_element_type=jnp.float32,
    )
    q_ridge = jnp.sum(ridge[None, :] * items * items, axis=1)
    lin = jnp.dot(items, theta, precision=highest, preferred_element_type=jnp.float32)
    packed = lax.psum(jnp.concatenate([z_part, q_ridge[None, :], lin[None, :]], axis=0), "col")
    rows_global = row_pos * width_row + lax.broadcasted_iota(jnp.int32, (width_row, width_col), 0)
    cols_global = col_pos * width_col + lax.broadcasted_iota(jnp.int32, (width_row, width_col), 1)
    tile = tile + jnp.where(rows_global == cols_global, ridge[None, :], jnp.float32(0.0))

    packed, tile = lax.optimization_barrier((packed, tile))
    ev_all = z_part.shape[0]
    z = packed[:ev_all]
    quad = jnp.sum(z * z, axis=0) + packed[ev_all]
    item_scores = packed[ev_all + 1] + jnp.sqrt(quad / F)
    items_dev = items.shape[0]
    held = item_scores
    step = 1
    while step < n_row:
        pairs = [(r, r ^ step) for r in range(n_row)]
        other = lax.ppermute(held, "row", pairs)
        low = (row_pos & step) == 0
        held = jnp.where(low, jnp.concatenate([held, other]), jnp.concatenate([other, held]))
        step *= 2
    scores = held[cand_ids]
    return (tile, scores)


def solution(mesh):
    return jax.shard_map(
        body,
        mesh=mesh,
        in_specs=(P("row", "col"), P(), P("col"), P("row", "col"), P(), P("col")),
        out_specs=(P("row", "col"), P()),
        check_vma=False,
    )
```

```python
import jax
import jax.numpy as jnp
from jax import lax
from jax.sharding import PartitionSpec as P

F = 16384

highest = lax.Precision.HIGHEST
high = lax.Precision.HIGH


def body(shared_rows, event_counts, ridge, items, cand_ids, theta):
    n_row = lax.axis_size("row")
    n_col = lax.axis_size("col")
    ratio = n_row // n_col
    row_pos = lax.axis_index("row")
    col_pos = lax.axis_index("col")
    ev_slots, width_col = shared_rows.shape
    width_row = width_col // ratio
    slot = lax.iota(jnp.int32, ev_slots)
    masked = jnp.where((slot < event_counts[row_pos])[:, None], shared_rows, jnp.float32(0.0))

    col_all = lax.all_gather(masked, "row", axis=0, tiled=True)

    halves = masked.reshape(ev_slots, ratio, width_row)
    received = []
    for t in range(ratio):
        perm = []
        for s in range(n_row):
            for c in range(n_col):
                b = (s % ratio) ^ t
                perm.append((s * n_col + c, (ratio * c + b) * n_col + s // ratio))
        piece = halves[:, (row_pos % ratio) ^ t, :]
        received.append(lax.ppermute(piece, ("row", "col"), perm))
    parity = row_pos % ratio
    ordered = [
        sum(jnp.where(parity ^ t == a, received[t], 0.0) for t in range(ratio))
        for a in range(ratio)
    ]
    row_block = jnp.concatenate(ordered, axis=0)

    n_y = n_col // 2
    ring = [y * 2 for y in range(n_y)] + [y * 2 + 1 for y in reversed(range(n_y))]
    where_in_ring = [ring.index(c) for c in range(n_col)]
    forward = [(ring[p], ring[(p + 1) % n_col]) for p in range(n_col)]
    backward = [(ring[p], ring[(p - 1) % n_col]) for p in range(n_col)]
    block_rows = row_block.shape[0]
    ring_tab = jnp.array(ring, jnp.int32)
    me = jnp.array(where_in_ring, jnp.int32)[col_pos]
    row_all = jnp.zeros((n_col * block_rows, width_row), jnp.float32)
    row_all = lax.dynamic_update_slice_in_dim(row_all, row_block, col_pos * block_rows, 0)
    ahead = behind = row_block
    for k in range(1, n_col // 2 + 1):
        ahead = lax.ppermute(ahead, "col", forward)
        row_all = lax.dynamic_update_slice_in_dim(
            row_all, ahead, ring_tab[(me - k) % n_col] * block_rows, 0
        )
        if k < n_col // 2:
            behind = lax.ppermute(behind, "col", backward)
            row_all = lax.dynamic_update_slice_in_dim(
                row_all, behind, ring_tab[(me + k) % n_col] * block_rows, 0
            )

    col_all, row_all = lax.optimization_barrier((col_all, row_all))
    contract = (((0,), (0,)), ((), ()))
    def rows_of_tile(lo, hi):
        return lax.dot_general(
            row_all[:, lo:hi], col_all, contract, precision=high,
            preferred_element_type=jnp.float32,
        )

    n_parts = 2
    part_rows = width_row // n_parts
    parts = []
    z_part = lax.dot_general(
        col_all, items, (((1,), (1,)), ((), ())), precision=high,
        preferred_element_type=jnp.float32,
    )
    q_ridge = jnp.sum(ridge[None, :] * items * items, axis=1)
    lin = jnp.dot(items, theta, precision=highest, preferred_element_type=jnp.float32)
    cur = z_part
    step = n_col // 2
    while step >= 1:
        pairs = [(c, c ^ step) for c in range(n_col)]
        rows_half = cur.shape[0] // 2
        lo_half, hi_half = cur[:rows_half], cur[rows_half:]
        upper = (col_pos & step) != 0
        keep = jnp.where(upper, hi_half, lo_half)
        send = jnp.where(upper, lo_half, hi_half)
        cur = keep + lax.ppermute(send, "col", pairs)
        if len(parts) < n_parts:
            lo = len(parts) * part_rows
            part = rows_of_tile(lo, lo + part_rows)
            part, cur = lax.optimization_barrier((part, cur))
            parts.append(part)
        step //= 2
    small = jnp.stack([jnp.sum(cur * cur, axis=0), q_ridge, lin])
    step = n_col // 2
    while step >= 1:
        pairs = [(c, c ^ step) for c in range(n_col)]
        small = small + lax.ppermute(small, "col", pairs)
        step //= 2
    tile = jnp.concatenate(parts, axis=0)
    rows_global = row_pos * width_row + lax.broadcasted_iota(jnp.int32, (width_row, width_col), 0)
    cols_global = col_pos * width_col + lax.broadcasted_iota(jnp.int32, (width_row, width_col), 1)
    tile = tile + jnp.where(rows_global == cols_global, ridge[None, :], jnp.float32(0.0))

    quad = small[0] + small[1]
    item_scores = small[2] + jnp.sqrt(quad / F)
    items_dev = items.shape[0]
    held = item_scores
    step = 1
    while step < n_row:
        pairs = [(r, r ^ step) for r in range(n_row)]
        other = lax.ppermute(held, "row", pairs)
        low = (row_pos & step) == 0
        held = jnp.where(low, jnp.concatenate([held, other]), jnp.concatenate([other, held]))
        step *= 2
    scores = held[cand_ids]
    return (tile, scores)


def solution(mesh):
    return jax.shard_map(
        body,
        mesh=mesh,
        in_specs=(P("row", "col"), P(), P("col"), P("row", "col"), P(), P("col")),
        out_specs=(P("row", "col"), P()),
        check_vma=False,
    )
```

```python
import jax
import jax.numpy as jnp
from jax import lax
from jax.sharding import PartitionSpec as P

F = 16384

highest = lax.Precision.HIGHEST
high = lax.Precision.HIGH


def body(shared_rows, event_counts, ridge, items, cand_ids, theta):
    n_row = lax.axis_size("row")
    n_col = lax.axis_size("col")
    ratio = n_row // n_col
    row_pos = lax.axis_index("row")
    col_pos = lax.axis_index("col")
    ev_slots, width_col = shared_rows.shape
    width_row = width_col // ratio
    slot = lax.iota(jnp.int32, ev_slots)
    masked = jnp.where((slot < event_counts[row_pos])[:, None], shared_rows, jnp.float32(0.0))

    col_all = lax.all_gather(masked, "row", axis=0, tiled=True)

    halves = masked.reshape(ev_slots, ratio, width_row)
    received = []
    for t in range(ratio):
        perm = []
        for s in range(n_row):
            for c in range(n_col):
                b = (s % ratio) ^ t
                perm.append((s * n_col + c, (ratio * c + b) * n_col + s // ratio))
        piece = halves[:, (row_pos % ratio) ^ t, :]
        received.append(lax.ppermute(piece, ("row", "col"), perm))
    parity = row_pos % ratio
    ordered = [
        sum(jnp.where(parity ^ t == a, received[t], 0.0) for t in range(ratio))
        for a in range(ratio)
    ]
    row_block = jnp.concatenate(ordered, axis=0)

    n_y = n_col // 2
    ring = [y * 2 for y in range(n_y)] + [y * 2 + 1 for y in reversed(range(n_y))]
    where_in_ring = [ring.index(c) for c in range(n_col)]
    forward = [(ring[p], ring[(p + 1) % n_col]) for p in range(n_col)]
    backward = [(ring[p], ring[(p - 1) % n_col]) for p in range(n_col)]
    block_rows = row_block.shape[0]
    half_rows = block_rows // 2
    ring_tab = jnp.array(ring, jnp.int32)
    me = jnp.array(where_in_ring, jnp.int32)[col_pos]
    row_all = jnp.zeros((n_col * block_rows, width_row), jnp.float32)
    ahead, behind = row_block[:half_rows], row_block[half_rows:]
    row_all = lax.dynamic_update_slice_in_dim(row_all, ahead, col_pos * block_rows, 0)
    row_all = lax.dynamic_update_slice_in_dim(row_all, behind, col_pos * block_rows + half_rows, 0)
    for k in range(1, n_col):
        ahead = lax.ppermute(ahead, "col", forward)
        behind = lax.ppermute(behind, "col", backward)
        from_ahead = ring_tab[(me - k) % n_col]
        from_behind = ring_tab[(me + k) % n_col]
        row_all = lax.dynamic_update_slice_in_dim(row_all, ahead, from_ahead * block_rows, 0)
        row_all = lax.dynamic_update_slice_in_dim(
            row_all, behind, from_behind * block_rows + half_rows, 0
        )

    z_part = lax.dot_general(
        col_all, items, (((1,), (1,)), ((), ())), precision=high,
        preferred_element_type=jnp.float32,
    )
    q_ridge = jnp.sum(ridge[None, :] * items * items, axis=1)
    lin = jnp.dot(items, theta, precision=highest, preferred_element_type=jnp.float32)
    packed = jnp.concatenate([z_part, q_ridge[None, :], lin[None, :]], axis=0)
    step = n_col // 2
    while step >= 1:
        pairs = [(c, c ^ step) for c in range(n_col)]
        packed = packed + lax.ppermute(packed, "col", pairs)
        step //= 2
    ev_all = z_part.shape[0]
    z = packed[:ev_all]
    quad = jnp.sum(z * z, axis=0) + packed[ev_all]
    item_scores = packed[ev_all + 1] + jnp.sqrt(quad / F)
    items_dev = items.shape[0]
    held = item_scores
    step = 1
    while step < n_row:
        pairs = [(r, r ^ step) for r in range(n_row)]
        other = lax.ppermute(held, "row", pairs)
        low = (row_pos & step) == 0
        held = jnp.where(low, jnp.concatenate([held, other]), jnp.concatenate([other, held]))
        step *= 2
    scores = held[cand_ids]
    row_all, scores = lax.optimization_barrier((row_all, scores))
    contract = (((0,), (0,)), ((), ()))
    tile = lax.dot_general(
        row_all, col_all, contract, precision=high, preferred_element_type=jnp.float32
    )
    rows_global = row_pos * width_row + lax.broadcasted_iota(jnp.int32, (width_row, width_col), 0)
    cols_global = col_pos * width_col + lax.broadcasted_iota(jnp.int32, (width_row, width_col), 1)
    tile = tile + jnp.where(rows_global == cols_global, ridge[None, :], jnp.float32(0.0))

    return (tile, scores)


def solution(mesh):
    return jax.shard_map(
        body,
        mesh=mesh,
        in_specs=(P("row", "col"), P(), P("col"), P("row", "col"), P(), P("col")),
        out_specs=(P("row", "col"), P()),
        check_vma=False,
    )
```

```python
import jax
import jax.numpy as jnp
from jax import lax
from jax.sharding import PartitionSpec as P

F = 16384

highest = lax.Precision.HIGHEST
high = lax.Precision.HIGH


def body(shared_rows, event_counts, ridge, items, cand_ids, theta):
    n_row = lax.axis_size("row")
    n_col = lax.axis_size("col")
    ratio = n_row // n_col
    row_pos = lax.axis_index("row")
    col_pos = lax.axis_index("col")
    ev_slots, width_col = shared_rows.shape
    width_row = width_col // ratio
    slot = lax.iota(jnp.int32, ev_slots)
    masked = jnp.where((slot < event_counts[row_pos])[:, None], shared_rows, jnp.float32(0.0))


    halves = masked.reshape(ev_slots, ratio, width_row)
    received = []
    for t in range(ratio):
        perm = []
        for s in range(n_row):
            for c in range(n_col):
                b = (s % ratio) ^ t
                perm.append((s * n_col + c, (ratio * c + b) * n_col + s // ratio))
        piece = halves[:, (row_pos % ratio) ^ t, :]
        received.append(lax.ppermute(piece, ("row", "col"), perm))
    parity = row_pos % ratio
    ordered = [
        sum(jnp.where(parity ^ t == a, received[t], 0.0) for t in range(ratio))
        for a in range(ratio)
    ]
    row_block = jnp.concatenate(ordered, axis=0)

    n_y = n_col // 2
    ring = [y * 2 for y in range(n_y)] + [y * 2 + 1 for y in reversed(range(n_y))]
    where_in_ring = [ring.index(c) for c in range(n_col)]
    forward = [(ring[p], ring[(p + 1) % n_col]) for p in range(n_col)]
    backward = [(ring[p], ring[(p - 1) % n_col]) for p in range(n_col)]
    block_rows = row_block.shape[0]
    half_rows = block_rows // 2
    ring_tab = jnp.array(ring, jnp.int32)
    me = jnp.array(where_in_ring, jnp.int32)[col_pos]
    row_all = jnp.zeros((n_col * block_rows, width_row), jnp.float32)
    ahead, behind = row_block[:half_rows], row_block[half_rows:]
    row_all = lax.dynamic_update_slice_in_dim(row_all, ahead, col_pos * block_rows, 0)
    row_all = lax.dynamic_update_slice_in_dim(row_all, behind, col_pos * block_rows + half_rows, 0)
    for k in range(1, n_col):
        ahead = lax.ppermute(ahead, "col", forward)
        behind = lax.ppermute(behind, "col", backward)
        if k == 1:
            gather_from, ahead, behind = lax.optimization_barrier((masked, ahead, behind))
            col_all = lax.all_gather(gather_from, "row", axis=0, tiled=True)
        from_ahead = ring_tab[(me - k) % n_col]
        from_behind = ring_tab[(me + k) % n_col]
        row_all = lax.dynamic_update_slice_in_dim(row_all, ahead, from_ahead * block_rows, 0)
        row_all = lax.dynamic_update_slice_in_dim(
            row_all, behind, from_behind * block_rows + half_rows, 0
        )

    z_part = lax.dot_general(
        col_all, items, (((1,), (1,)), ((), ())), precision=high,
        preferred_element_type=jnp.float32,
    )
    q_ridge = jnp.sum(ridge[None, :] * items * items, axis=1)
    lin = jnp.dot(items, theta, precision=highest, preferred_element_type=jnp.float32)
    packed = jnp.concatenate([z_part, q_ridge[None, :], lin[None, :]], axis=0)
    step = n_col // 2
    while step >= 1:
        pairs = [(c, c ^ step) for c in range(n_col)]
        packed = packed + lax.ppermute(packed, "col", pairs)
        step //= 2
    ev_all = z_part.shape[0]
    z = packed[:ev_all]
    quad = jnp.sum(z * z, axis=0) + packed[ev_all]
    item_scores = packed[ev_all + 1] + jnp.sqrt(quad / F)
    items_dev = items.shape[0]
    held = item_scores
    step = 1
    while step < n_row:
        pairs = [(r, r ^ step) for r in range(n_row)]
        other = lax.ppermute(held, "row", pairs)
        low = (row_pos & step) == 0
        held = jnp.where(low, jnp.concatenate([held, other]), jnp.concatenate([other, held]))
        step *= 2
    scores = held[cand_ids]
    row_all, scores = lax.optimization_barrier((row_all, scores))
    contract = (((0,), (0,)), ((), ()))
    tile = lax.dot_general(
        row_all, col_all, contract, precision=high, preferred_element_type=jnp.float32
    )
    rows_global = row_pos * width_row + lax.broadcasted_iota(jnp.int32, (width_row, width_col), 0)
    cols_global = col_pos * width_col + lax.broadcasted_iota(jnp.int32, (width_row, width_col), 1)
    tile = tile + jnp.where(rows_global == cols_global, ridge[None, :], jnp.float32(0.0))

    return (tile, scores)


def solution(mesh):
    return jax.shard_map(
        body,
        mesh=mesh,
        in_specs=(P("row", "col"), P(), P("col"), P("row", "col"), P(), P("col")),
        out_specs=(P("row", "col"), P()),
        check_vma=False,
    )
```

```python
import jax
import jax.numpy as jnp
from jax import lax
from jax.sharding import PartitionSpec as P

F = 16384

highest = lax.Precision.HIGHEST
high = lax.Precision.HIGH


def body(shared_rows, event_counts, ridge, items, cand_ids, theta):
    n_row = lax.axis_size("row")
    n_col = lax.axis_size("col")
    ratio = n_row // n_col
    row_pos = lax.axis_index("row")
    col_pos = lax.axis_index("col")
    ev_slots, width_col = shared_rows.shape
    width_row = width_col // ratio
    slot = lax.iota(jnp.int32, ev_slots)
    masked = jnp.where((slot < event_counts[row_pos])[:, None], shared_rows, jnp.float32(0.0))

    col_all = lax.all_gather(masked, "row", axis=0, tiled=True)

    halves = masked.reshape(ev_slots, ratio, width_row)
    received = []
    for t in range(ratio):
        perm = []
        for s in range(n_row):
            for c in range(n_col):
                b = (s % ratio) ^ t
                perm.append((s * n_col + c, (ratio * c + b) * n_col + s // ratio))
        piece = halves[:, (row_pos % ratio) ^ t, :]
        received.append(lax.ppermute(piece, ("row", "col"), perm))
    parity = row_pos % ratio
    ordered = [
        sum(jnp.where(parity ^ t == a, received[t], 0.0) for t in range(ratio))
        for a in range(ratio)
    ]
    row_block = jnp.concatenate(ordered, axis=0)

    n_y = n_col // 2
    ring = [y * 2 for y in range(n_y)] + [y * 2 + 1 for y in reversed(range(n_y))]
    where_in_ring = [ring.index(c) for c in range(n_col)]
    forward = [(ring[p], ring[(p + 1) % n_col]) for p in range(n_col)]
    backward = [(ring[p], ring[(p - 1) % n_col]) for p in range(n_col)]
    block_rows = row_block.shape[0]
    half_rows = block_rows // 2
    ring_tab = jnp.array(ring, jnp.int32)
    me = jnp.array(where_in_ring, jnp.int32)[col_pos]
    row_all = jnp.zeros((n_col * block_rows, width_row), jnp.float32)
    ahead, behind = row_block[:half_rows], row_block[half_rows:]
    row_all = lax.dynamic_update_slice_in_dim(row_all, ahead, col_pos * block_rows, 0)
    row_all = lax.dynamic_update_slice_in_dim(row_all, behind, col_pos * block_rows + half_rows, 0)
    for k in range(1, n_col):
        ahead = lax.ppermute(ahead, "col", forward)
        behind = lax.ppermute(behind, "col", backward)
        from_ahead = ring_tab[(me - k) % n_col]
        from_behind = ring_tab[(me + k) % n_col]
        if k == n_col - 1:
            break
        row_all = lax.dynamic_update_slice_in_dim(row_all, ahead, from_ahead * block_rows, 0)
        row_all = lax.dynamic_update_slice_in_dim(
            row_all, behind, from_behind * block_rows + half_rows, 0
        )

    z_part = lax.dot_general(
        col_all, items, (((1,), (1,)), ((), ())), precision=high,
        preferred_element_type=jnp.float32,
    )
    q_ridge = jnp.sum(ridge[None, :] * items * items, axis=1)
    lin = jnp.dot(items, theta, precision=highest, preferred_element_type=jnp.float32)
    packed = jnp.concatenate([z_part, q_ridge[None, :], lin[None, :]], axis=0)
    step = n_col // 2
    while step >= 1:
        pairs = [(c, c ^ step) for c in range(n_col)]
        packed = packed + lax.ppermute(packed, "col", pairs)
        step //= 2
    ev_all = z_part.shape[0]
    z = packed[:ev_all]
    quad = jnp.sum(z * z, axis=0) + packed[ev_all]
    item_scores = packed[ev_all + 1] + jnp.sqrt(quad / F)
    items_dev = items.shape[0]
    held = item_scores
    step = 1
    while step < n_row:
        pairs = [(r, r ^ step) for r in range(n_row)]
        other = lax.ppermute(held, "row", pairs)
        low = (row_pos & step) == 0
        held = jnp.where(low, jnp.concatenate([held, other]), jnp.concatenate([other, held]))
        step *= 2
    scores = held[cand_ids]
    row_all, scores = lax.optimization_barrier((row_all, scores))
    contract = (((0,), (0,)), ((), ()))
    tile = lax.dot_general(
        row_all, col_all, contract, precision=high, preferred_element_type=jnp.float32
    )
    last_rows = jnp.concatenate([ahead, behind], axis=0)
    last_cols = jnp.concatenate([
        lax.dynamic_slice_in_dim(col_all, from_ahead * block_rows, half_rows, 0),
        lax.dynamic_slice_in_dim(col_all, from_behind * block_rows + half_rows, half_rows, 0),
    ], axis=0)
    tile = tile + lax.dot_general(
        last_rows, last_cols, contract, precision=high, preferred_element_type=jnp.float32
    )
    rows_global = row_pos * width_row + lax.broadcasted_iota(jnp.int32, (width_row, width_col), 0)
    cols_global = col_pos * width_col + lax.broadcasted_iota(jnp.int32, (width_row, width_col), 1)
    tile = tile + jnp.where(rows_global == cols_global, ridge[None, :], jnp.float32(0.0))

    return (tile, scores)


def solution(mesh):
    return jax.shard_map(
        body,
        mesh=mesh,
        in_specs=(P("row", "col"), P(), P("col"), P("row", "col"), P(), P("col")),
        out_specs=(P("row", "col"), P()),
        check_vma=False,
    )
```

```python
import jax
import jax.numpy as jnp
from jax import lax
from jax.sharding import PartitionSpec as P

F = 16384

highest = lax.Precision.HIGHEST
high = lax.Precision.HIGH


def body(shared_rows, event_counts, ridge, items, cand_ids, theta):
    n_row = lax.axis_size("row")
    n_col = lax.axis_size("col")
    ratio = n_row // n_col
    row_pos = lax.axis_index("row")
    col_pos = lax.axis_index("col")
    ev_slots, width_col = shared_rows.shape
    width_row = width_col // ratio
    slot = lax.iota(jnp.int32, ev_slots)
    masked = jnp.where((slot < event_counts[row_pos])[:, None], shared_rows, jnp.float32(0.0))

    col_all = lax.all_gather(masked, "row", axis=0, tiled=True)

    halves = masked.reshape(ev_slots, ratio, width_row)
    received = []
    for t in range(ratio):
        perm = []
        for s in range(n_row):
            for c in range(n_col):
                b = (s % ratio) ^ t
                perm.append((s * n_col + c, (ratio * c + b) * n_col + s // ratio))
        piece = halves[:, (row_pos % ratio) ^ t, :]
        received.append(lax.ppermute(piece, ("row", "col"), perm))
    parity = row_pos % ratio
    ordered = [
        sum(jnp.where(parity ^ t == a, received[t], 0.0) for t in range(ratio))
        for a in range(ratio)
    ]
    row_block = jnp.concatenate(ordered, axis=0)

    n_y = n_col // 2
    ring = [y * 2 for y in range(n_y)] + [y * 2 + 1 for y in reversed(range(n_y))]
    where_in_ring = [ring.index(c) for c in range(n_col)]
    pairs = []
    for r in range(n_row):
        way = 1 if r % 2 == 0 else -1
        for p in range(n_col):
            pairs.append((r * n_col + ring[p], r * n_col + ring[(p + way) % n_col]))
    block_rows = row_block.shape[0]
    ring_tab = jnp.array(ring, jnp.int32)
    me = jnp.array(where_in_ring, jnp.int32)[col_pos]
    way = 1 - 2 * (row_pos % 2)
    row_all = jnp.zeros((n_col * block_rows, width_row), jnp.float32)
    row_all = lax.dynamic_update_slice_in_dim(row_all, row_block, col_pos * block_rows, 0)
    held = row_block
    for k in range(1, n_col):
        held = lax.ppermute(held, ("row", "col"), pairs)
        came_from = ring_tab[(me - k * way) % n_col]
        row_all = lax.dynamic_update_slice_in_dim(row_all, held, came_from * block_rows, 0)

    z_part = lax.dot_general(
        col_all, items, (((1,), (1,)), ((), ())), precision=high,
        preferred_element_type=jnp.float32,
    )
    q_ridge = jnp.sum(ridge[None, :] * items * items, axis=1)
    lin = jnp.dot(items, theta, precision=highest, preferred_element_type=jnp.float32)
    packed = jnp.concatenate([z_part, q_ridge[None, :], lin[None, :]], axis=0)
    step = n_col // 2
    while step >= 1:
        pairs = [(c, c ^ step) for c in range(n_col)]
        packed = packed + lax.ppermute(packed, "col", pairs)
        step //= 2
    ev_all = z_part.shape[0]
    z = packed[:ev_all]
    quad = jnp.sum(z * z, axis=0) + packed[ev_all]
    item_scores = packed[ev_all + 1] + jnp.sqrt(quad / F)
    items_dev = items.shape[0]
    held = item_scores
    step = 1
    while step < n_row:
        pairs = [(r, r ^ step) for r in range(n_row)]
        other = lax.ppermute(held, "row", pairs)
        low = (row_pos & step) == 0
        held = jnp.where(low, jnp.concatenate([held, other]), jnp.concatenate([other, held]))
        step *= 2
    scores = held[cand_ids]
    row_all, scores = lax.optimization_barrier((row_all, scores))
    contract = (((0,), (0,)), ((), ()))
    tile = lax.dot_general(
        row_all, col_all, contract, precision=high, preferred_element_type=jnp.float32
    )
    rows_global = row_pos * width_row + lax.broadcasted_iota(jnp.int32, (width_row, width_col), 0)
    cols_global = col_pos * width_col + lax.broadcasted_iota(jnp.int32, (width_row, width_col), 1)
    tile = tile + jnp.where(rows_global == cols_global, ridge[None, :], jnp.float32(0.0))

    return (tile, scores)


def solution(mesh):
    return jax.shard_map(
        body,
        mesh=mesh,
        in_specs=(P("row", "col"), P(), P("col"), P("row", "col"), P(), P("col")),
        out_specs=(P("row", "col"), P()),
        check_vma=False,
    )
```

```python
import jax
import jax.numpy as jnp
from jax import lax
from jax.sharding import PartitionSpec as P

F = 16384

highest = lax.Precision.HIGHEST
high = lax.Precision.HIGH


def body(shared_rows, event_counts, ridge, items, cand_ids, theta):
    n_row = lax.axis_size("row")
    n_col = lax.axis_size("col")
    ratio = n_row // n_col
    row_pos = lax.axis_index("row")
    col_pos = lax.axis_index("col")
    ev_slots, width_col = shared_rows.shape
    width_row = width_col // ratio
    slot = lax.iota(jnp.int32, ev_slots)
    masked = jnp.where((slot < event_counts[row_pos])[:, None], shared_rows, jnp.float32(0.0))

    col_all = lax.all_gather(masked, "row", axis=0, tiled=True)

    halves = masked.reshape(ev_slots, ratio, width_row)
    received = []
    for t in range(ratio):
        perm = []
        for s in range(n_row):
            for c in range(n_col):
                b = (s % ratio) ^ t
                perm.append((s * n_col + c, (ratio * c + b) * n_col + s // ratio))
        piece = halves[:, (row_pos % ratio) ^ t, :]
        received.append(lax.ppermute(piece, ("row", "col"), perm))
    parity = row_pos % ratio
    ordered = [
        sum(jnp.where(parity ^ t == a, received[t], 0.0) for t in range(ratio))
        for a in range(ratio)
    ]
    row_block = jnp.concatenate(ordered, axis=0)

    n_y = n_col // 2
    ring = [y * 2 for y in range(n_y)] + [y * 2 + 1 for y in reversed(range(n_y))]
    where_in_ring = [ring.index(c) for c in range(n_col)]
    pairs = []
    for r in range(n_row):
        way = 1 if r % 2 == 0 else -1
        for p in range(n_col):
            pairs.append((r * n_col + ring[p], r * n_col + ring[(p + way) % n_col]))
    block_rows = row_block.shape[0]
    ring_tab = jnp.array(ring, jnp.int32)
    me = jnp.array(where_in_ring, jnp.int32)[col_pos]
    way = 1 - 2 * (row_pos % 2)
    held = row_block
    for k in range(1, n_col):
        held = lax.ppermute(held, ("row", "col"), pairs)
        if k == 1:
            row_all, held = lax.optimization_barrier(
                (jnp.zeros((n_col * block_rows, width_row), jnp.float32), held)
            )
            row_all = lax.dynamic_update_slice_in_dim(row_all, row_block, col_pos * block_rows, 0)
        came_from = ring_tab[(me - k * way) % n_col]
        row_all = lax.dynamic_update_slice_in_dim(row_all, held, came_from * block_rows, 0)

    z_part = lax.dot_general(
        col_all, items, (((1,), (1,)), ((), ())), precision=high,
        preferred_element_type=jnp.float32,
    )
    q_ridge = jnp.sum(ridge[None, :] * items * items, axis=1)
    lin = jnp.dot(items, theta, precision=highest, preferred_element_type=jnp.float32)
    packed = jnp.concatenate([z_part, q_ridge[None, :], lin[None, :]], axis=0)
    step = n_col // 2
    while step >= 1:
        pairs = [(c, c ^ step) for c in range(n_col)]
        packed = packed + lax.ppermute(packed, "col", pairs)
        step //= 2
    ev_all = z_part.shape[0]
    z = packed[:ev_all]
    quad = jnp.sum(z * z, axis=0) + packed[ev_all]
    item_scores = packed[ev_all + 1] + jnp.sqrt(quad / F)
    items_dev = items.shape[0]
    held = item_scores
    step = 1
    while step < n_row:
        pairs = [(r, r ^ step) for r in range(n_row)]
        other = lax.ppermute(held, "row", pairs)
        low = (row_pos & step) == 0
        held = jnp.where(low, jnp.concatenate([held, other]), jnp.concatenate([other, held]))
        step *= 2
    scores = held[cand_ids]
    row_all, scores = lax.optimization_barrier((row_all, scores))
    contract = (((0,), (0,)), ((), ()))
    tile = lax.dot_general(
        row_all, col_all, contract, precision=high, preferred_element_type=jnp.float32
    )
    rows_global = row_pos * width_row + lax.broadcasted_iota(jnp.int32, (width_row, width_col), 0)
    cols_global = col_pos * width_col + lax.broadcasted_iota(jnp.int32, (width_row, width_col), 1)
    tile = tile + jnp.where(rows_global == cols_global, ridge[None, :], jnp.float32(0.0))

    return (tile, scores)


def solution(mesh):
    return jax.shard_map(
        body,
        mesh=mesh,
        in_specs=(P("row", "col"), P(), P("col"), P("row", "col"), P(), P("col")),
        out_specs=(P("row", "col"), P()),
        check_vma=False,
    )
```

```python
import jax
import jax.numpy as jnp
from jax import lax
from jax.sharding import PartitionSpec as P

F = 16384

highest = lax.Precision.HIGHEST
high = lax.Precision.HIGH


def body(shared_rows, event_counts, ridge, items, cand_ids, theta):
    n_row = lax.axis_size("row")
    n_col = lax.axis_size("col")
    ratio = n_row // n_col
    row_pos = lax.axis_index("row")
    col_pos = lax.axis_index("col")
    ev_slots, width_col = shared_rows.shape
    width_row = width_col // ratio
    slot = lax.iota(jnp.int32, ev_slots)
    masked = jnp.where((slot < event_counts[row_pos])[:, None], shared_rows, jnp.float32(0.0))

    col_all = lax.all_gather(masked, "row", axis=0, tiled=True)

    halves = masked.reshape(ev_slots, ratio, width_row)
    received = []
    for t in range(ratio):
        perm = []
        for s in range(n_row):
            for c in range(n_col):
                b = (s % ratio) ^ t
                perm.append((s * n_col + c, (ratio * c + b) * n_col + s // ratio))
        piece = halves[:, (row_pos % ratio) ^ t, :]
        received.append(lax.ppermute(piece, ("row", "col"), perm))
    parity = row_pos % ratio
    ordered = [
        sum(jnp.where(parity ^ t == a, received[t], 0.0) for t in range(ratio))
        for a in range(ratio)
    ]
    row_block = jnp.concatenate(ordered, axis=0)

    n_y = n_col // 2
    ring = [y * 2 for y in range(n_y)] + [y * 2 + 1 for y in reversed(range(n_y))]
    where_in_ring = [ring.index(c) for c in range(n_col)]
    pairs = []
    for r in range(n_row):
        way = 1 if r % 2 == 0 else -1
        for p in range(n_col):
            pairs.append((r * n_col + ring[p], r * n_col + ring[(p + way) % n_col]))
    block_rows = row_block.shape[0]
    ring_tab = jnp.array(ring, jnp.int32)
    me = jnp.array(where_in_ring, jnp.int32)[col_pos]
    way = 1 - 2 * (row_pos % 2)
    held = row_block
    for k in range(1, n_col):
        held = lax.ppermute(held, ("row", "col"), pairs)
        if k == 1:
            row_all, held = lax.optimization_barrier(
                (jnp.zeros((n_col * block_rows, width_row), jnp.float32), held)
            )
            row_all = lax.dynamic_update_slice_in_dim(row_all, row_block, col_pos * block_rows, 0)
        came_from = ring_tab[(me - k * way) % n_col]
        row_all = lax.dynamic_update_slice_in_dim(row_all, held, came_from * block_rows, 0)

    z_part = lax.dot_general(
        col_all, items, (((1,), (1,)), ((), ())), precision=high,
        preferred_element_type=jnp.float32,
    )
    q_ridge = jnp.sum(ridge[None, :] * items * items, axis=1)
    lin = jnp.dot(items, theta, precision=highest, preferred_element_type=jnp.float32)
    packed = jnp.concatenate([z_part, q_ridge[None, :], lin[None, :]], axis=0)
    step = n_col // 2
    while step >= 1:
        pairs = [(c, c ^ step) for c in range(n_col)]
        packed = packed + lax.ppermute(packed, "col", pairs)
        step //= 2
    ev_all = z_part.shape[0]
    z = packed[:ev_all]
    quad = jnp.sum(z * z, axis=0) + packed[ev_all]
    item_scores = packed[ev_all + 1] + jnp.sqrt(quad / F)
    items_dev = items.shape[0]
    held = item_scores
    step = 1
    while step < n_row:
        pairs = [(r, r ^ step) for r in range(n_row)]
        other = lax.ppermute(held, "row", pairs)
        low = (row_pos & step) == 0
        held = jnp.where(low, jnp.concatenate([held, other]), jnp.concatenate([other, held]))
        step *= 2
    pick = cand_ids[:, None] == lax.broadcasted_iota(jnp.int32, (cand_ids.shape[0], held.shape[0]), 1)
    scores = jnp.sum(jnp.where(pick, held[None, :], jnp.float32(0.0)), axis=1)
    row_all, scores = lax.optimization_barrier((row_all, scores))
    contract = (((0,), (0,)), ((), ()))
    tile = lax.dot_general(
        row_all, col_all, contract, precision=high, preferred_element_type=jnp.float32
    )
    rows_global = row_pos * width_row + lax.broadcasted_iota(jnp.int32, (width_row, width_col), 0)
    cols_global = col_pos * width_col + lax.broadcasted_iota(jnp.int32, (width_row, width_col), 1)
    tile = tile + jnp.where(rows_global == cols_global, ridge[None, :], jnp.float32(0.0))

    return (tile, scores)


def solution(mesh):
    return jax.shard_map(
        body,
        mesh=mesh,
        in_specs=(P("row", "col"), P(), P("col"), P("row", "col"), P(), P("col")),
        out_specs=(P("row", "col"), P()),
        check_vma=False,
    )
```

```python
import jax
import jax.numpy as jnp
from jax import lax
from jax.sharding import PartitionSpec as P

F = 16384

highest = lax.Precision.HIGHEST
high = lax.Precision.HIGH


def body(shared_rows, event_counts, ridge, items, cand_ids, theta):
    n_row = lax.axis_size("row")
    n_col = lax.axis_size("col")
    ratio = n_row // n_col
    row_pos = lax.axis_index("row")
    col_pos = lax.axis_index("col")
    ev_slots, width_col = shared_rows.shape
    width_row = width_col // ratio
    slot = lax.iota(jnp.int32, ev_slots)
    masked = jnp.where((slot < event_counts[row_pos])[:, None], shared_rows, jnp.float32(0.0))

    col_all = lax.all_gather(masked, "row", axis=0, tiled=True)

    received = []
    for t in range(ratio):
        perm = []
        for s in range(n_row):
            for c in range(n_col):
                b = (s % ratio) ^ t
                perm.append((s * n_col + c, (ratio * c + b) * n_col + s // ratio))
        piece = lax.dynamic_slice_in_dim(masked, ((row_pos % ratio) ^ t) * width_row, width_row, 1)
        received.append(lax.ppermute(piece, ("row", "col"), perm))
    parity = row_pos % ratio
    ordered = [
        sum(jnp.where(parity ^ t == a, received[t], 0.0) for t in range(ratio))
        for a in range(ratio)
    ]
    row_block = jnp.concatenate(ordered, axis=0)

    n_y = n_col // 2
    ring = [y * 2 for y in range(n_y)] + [y * 2 + 1 for y in reversed(range(n_y))]
    where_in_ring = [ring.index(c) for c in range(n_col)]
    pairs = []
    for r in range(n_row):
        way = 1 if r % 2 == 0 else -1
        for p in range(n_col):
            pairs.append((r * n_col + ring[p], r * n_col + ring[(p + way) % n_col]))
    block_rows = row_block.shape[0]
    ring_tab = jnp.array(ring, jnp.int32)
    me = jnp.array(where_in_ring, jnp.int32)[col_pos]
    way = 1 - 2 * (row_pos % 2)
    held = row_block
    for k in range(1, n_col):
        held = lax.ppermute(held, ("row", "col"), pairs)
        if k == 1:
            row_all, held = lax.optimization_barrier(
                (jnp.zeros((n_col * block_rows, width_row), jnp.float32), held)
            )
            row_all = lax.dynamic_update_slice_in_dim(row_all, row_block, col_pos * block_rows, 0)
        came_from = ring_tab[(me - k * way) % n_col]
        row_all = lax.dynamic_update_slice_in_dim(row_all, held, came_from * block_rows, 0)

    z_part = lax.dot_general(
        col_all, items, (((1,), (1,)), ((), ())), precision=high,
        preferred_element_type=jnp.float32,
    )
    q_ridge = jnp.sum(ridge[None, :] * items * items, axis=1)
    lin = jnp.dot(items, theta, precision=highest, preferred_element_type=jnp.float32)
    packed = jnp.concatenate([z_part, q_ridge[None, :], lin[None, :]], axis=0)
    step = n_col // 2
    while step >= 1:
        pairs = [(c, c ^ step) for c in range(n_col)]
        packed = packed + lax.ppermute(packed, "col", pairs)
        step //= 2
    ev_all = z_part.shape[0]
    z = packed[:ev_all]
    quad = jnp.sum(z * z, axis=0) + packed[ev_all]
    item_scores = packed[ev_all + 1] + jnp.sqrt(quad / F)
    items_dev = items.shape[0]
    held = item_scores
    step = 1
    while step < n_row:
        pairs = [(r, r ^ step) for r in range(n_row)]
        other = lax.ppermute(held, "row", pairs)
        low = (row_pos & step) == 0
        held = jnp.where(low, jnp.concatenate([held, other]), jnp.concatenate([other, held]))
        step *= 2
    pick = cand_ids[:, None] == lax.broadcasted_iota(jnp.int32, (cand_ids.shape[0], held.shape[0]), 1)
    scores = jnp.sum(jnp.where(pick, held[None, :], jnp.float32(0.0)), axis=1)
    row_all, scores = lax.optimization_barrier((row_all, scores))
    contract = (((0,), (0,)), ((), ()))
    tile = lax.dot_general(
        row_all, col_all, contract, precision=high, preferred_element_type=jnp.float32
    )
    rows_global = row_pos * width_row + lax.broadcasted_iota(jnp.int32, (width_row, width_col), 0)
    cols_global = col_pos * width_col + lax.broadcasted_iota(jnp.int32, (width_row, width_col), 1)
    tile = tile + jnp.where(rows_global == cols_global, ridge[None, :], jnp.float32(0.0))

    return (tile, scores)


def solution(mesh):
    return jax.shard_map(
        body,
        mesh=mesh,
        in_specs=(P("row", "col"), P(), P("col"), P("row", "col"), P(), P("col")),
        out_specs=(P("row", "col"), P()),
        check_vma=False,
    )
```

```python
import jax
import jax.numpy as jnp
from jax import lax
from jax.sharding import PartitionSpec as P

F = 16384

highest = lax.Precision.HIGHEST
high = lax.Precision.HIGH


def body(shared_rows, event_counts, ridge, items, cand_ids, theta):
    n_row = lax.axis_size("row")
    n_col = lax.axis_size("col")
    ratio = n_row // n_col
    row_pos = lax.axis_index("row")
    col_pos = lax.axis_index("col")
    ev_slots, width_col = shared_rows.shape
    width_row = width_col // ratio
    slot = lax.iota(jnp.int32, ev_slots)
    masked = jnp.where((slot < event_counts[row_pos])[:, None], shared_rows, jnp.float32(0.0))

    col_all = lax.all_gather(masked, "row", axis=0, tiled=True)

    received = []
    for t in range(ratio):
        perm = []
        for s in range(n_row):
            for c in range(n_col):
                b = (s % ratio) ^ t
                perm.append((s * n_col + c, (ratio * c + b) * n_col + s // ratio))
        piece = lax.dynamic_slice_in_dim(masked, ((row_pos % ratio) ^ t) * width_row, width_row, 1)
        received.append(lax.ppermute(piece, ("row", "col"), perm))
    parity = row_pos % ratio
    row_block = jnp.where(
        parity == 0,
        jnp.concatenate([received[0], received[1]], axis=0),
        jnp.concatenate([received[1], received[0]], axis=0),
    )

    n_y = n_col // 2
    ring = [y * 2 for y in range(n_y)] + [y * 2 + 1 for y in reversed(range(n_y))]
    where_in_ring = [ring.index(c) for c in range(n_col)]
    pairs = []
    for r in range(n_row):
        way = 1 if r % 2 == 0 else -1
        for p in range(n_col):
            pairs.append((r * n_col + ring[p], r * n_col + ring[(p + way) % n_col]))
    block_rows = row_block.shape[0]
    ring_tab = jnp.array(ring, jnp.int32)
    me = jnp.array(where_in_ring, jnp.int32)[col_pos]
    way = 1 - 2 * (row_pos % 2)
    held = row_block
    for k in range(1, n_col):
        held = lax.ppermute(held, ("row", "col"), pairs)
        if k == 1:
            row_all, held = lax.optimization_barrier(
                (jnp.zeros((n_col * block_rows, width_row), jnp.float32), held)
            )
            row_all = lax.dynamic_update_slice_in_dim(row_all, row_block, col_pos * block_rows, 0)
        came_from = ring_tab[(me - k * way) % n_col]
        row_all = lax.dynamic_update_slice_in_dim(row_all, held, came_from * block_rows, 0)

    z_part = lax.dot_general(
        col_all, items, (((1,), (1,)), ((), ())), precision=high,
        preferred_element_type=jnp.float32,
    )
    q_ridge = jnp.sum(ridge[None, :] * items * items, axis=1)
    lin = jnp.dot(items, theta, precision=highest, preferred_element_type=jnp.float32)
    packed = jnp.concatenate([z_part, q_ridge[None, :], lin[None, :]], axis=0)
    step = n_col // 2
    while step >= 1:
        pairs = [(c, c ^ step) for c in range(n_col)]
        packed = packed + lax.ppermute(packed, "col", pairs)
        step //= 2
    ev_all = z_part.shape[0]
    z = packed[:ev_all]
    quad = jnp.sum(z * z, axis=0) + packed[ev_all]
    item_scores = packed[ev_all + 1] + jnp.sqrt(quad / F)
    items_dev = items.shape[0]
    held = item_scores
    step = 1
    while step < n_row:
        pairs = [(r, r ^ step) for r in range(n_row)]
        other = lax.ppermute(held, "row", pairs)
        low = (row_pos & step) == 0
        held = jnp.where(low, jnp.concatenate([held, other]), jnp.concatenate([other, held]))
        step *= 2
    pick = cand_ids[:, None] == lax.broadcasted_iota(jnp.int32, (cand_ids.shape[0], held.shape[0]), 1)
    scores = jnp.sum(jnp.where(pick, held[None, :], jnp.float32(0.0)), axis=1)
    row_all, scores = lax.optimization_barrier((row_all, scores))
    contract = (((0,), (0,)), ((), ()))
    tile = lax.dot_general(
        row_all, col_all, contract, precision=high, preferred_element_type=jnp.float32
    )
    rows_global = row_pos * width_row + lax.broadcasted_iota(jnp.int32, (width_row, width_col), 0)
    cols_global = col_pos * width_col + lax.broadcasted_iota(jnp.int32, (width_row, width_col), 1)
    tile = tile + jnp.where(rows_global == cols_global, ridge[None, :], jnp.float32(0.0))

    return (tile, scores)


def solution(mesh):
    return jax.shard_map(
        body,
        mesh=mesh,
        in_specs=(P("row", "col"), P(), P("col"), P("row", "col"), P(), P("col")),
        out_specs=(P("row", "col"), P()),
        check_vma=False,
    )
```
